512 devices in a mesh: tm: 128 (over z, y, core), chan: 4 (over x).
Axes of the slice: x: 4, y: 4, z: 16, core: 2. Of those that a mesh axis runs over, the one named last changes fastest.
Arguments:
- series: bfloat16 [32768, 512], P('tm', 'chan'), may hold values from -6 to 6
- proj_weight: bfloat16 [512, 3, 512], P(None, None, 'chan'), may hold values from -0.25 to 0.25
- proj_bias: float32 [3, 512], P(None, 'chan'), may hold values from -6 to 6
- short_taps: float32 [3, 3, 512], P(None, None, 'chan'), may hold values from -6 to 6
- short_bias: float32 [3, 512], P(None, 'chan'), may hold values from -6 to 6
- spectrum: float32 [2, 128, 2, 256, 512], P(None, 'tm', None, None, 'chan'), may hold values from -6 to 6
- skip_gain: float32 [512], P('chan'), may hold values from -6 to 6
- out_weight: bfloat16 [512, 512], replicated, may hold values from -0.25 to 0.25
- out_bias: float32 [512], P('chan'), may hold values from -6 to 6
Outputs:
- mixed_out: bfloat16 [32768, 512], P('tm', 'chan')
The draws below stay inside these ranges and needn't reach their ends.
All inputs are finite; a program needn't handle non-finite values.
Results may differ from the reference program's by a relative error of at most 0.009.
Values may be sent and summed in bfloat16 or wider, within the bound.
No kernel may reach another device: no remote copies, remote signals or barrier semaphores. Data moves between devices by JAX's collectives and lax.ppermute only.
A program may use at most 64 MiB of HBM per device.

```python
import jax
import jax.numpy as jnp
from jax import lax

D = 512
TM_DEV = 256
KS = 3
L = 32768
FFT = 65536
N_TM = 128


def block_scale(rng, shape, pieces, smallest, high):
    gain, own = 1.0, jax.random.fold_in(rng, 6)
    for position, parts in pieces:
        heights = jnp.exp(jax.random.uniform(jax.random.fold_in(own, position), (parts,), jnp.float32, smallest / len(pieces), high / len(pieces)))
        gain = gain * jnp.repeat(heights, shape[position] // parts).reshape([-1 if axis == position else 1 for axis in range(len(shape))])
    return gain


def noise(key, dims, scale, bound, pieces=(), held_as=jnp.bfloat16):
    array = jax.random.normal(key, dims, jnp.float32) * scale
    if len(pieces) > 0:
        array = block_scale(key, dims, pieces, -0.22, 0.18) * array
    return jnp.clip(array, min=-bound, max=bound).astype(held_as)


def setup_inputs(seed: int = 0) -> dict:
    key_of = jax.random.split(jax.random.key(seed), 10)
    series = noise(key_of[0], (L, D), 1.0, 6.0, ((0, 128), (1, 4)))
    proj_weight = noise(key_of[1], (D, 3, D), D ** -0.5, 0.25, ((2, 4),))
    proj_bias = noise(key_of[2], (3, D), 1.0, 6.0, ((1, 4),), jnp.float32)
    short_taps = noise(key_of[3], (KS, 3, D), 0.6, 6.0, ((2, 4),), jnp.float32)
    short_bias = noise(key_of[4], (3, D), 0.5, 6.0, ((1, 4),), jnp.float32)
    spectrum = noise(key_of[5], (2, N_TM, 2, TM_DEV, D), 1.2, 6.0, ((1, 128), (4, 4)), jnp.float32)
    skip_gain = noise(key_of[6], (D,), 1.0, 6.0, ((0, 4),), jnp.float32)
    out_weight = noise(key_of[7], (D, D), D ** -0.5, 0.25)
    out_bias = noise(key_of[8], (D,), 1.0, 6.0, ((0, 4),), jnp.float32)
    return dict(series=series, proj_weight=proj_weight, proj_bias=proj_bias, short_taps=short_taps, short_bias=short_bias, spectrum=spectrum, skip_gain=skip_gain, out_weight=out_weight, out_bias=out_bias)


def reverse_bits(values, digits):
    result = jnp.zeros_like(values)
    for bit_level in range(digits):
        result = result | (((values >> bit_level) & 1) << (digits - 1 - bit_level))
    return result


def reference(series, proj_weight, proj_bias, short_taps, short_bias, spectrum, skip_gain, out_weight, out_bias):
    length = series.shape[0]
    projected = jnp.dot(series, proj_weight.reshape(D, 3 * D), preferred_element_type=jnp.float32).reshape(length, 3, D)
    projected = lax.optimization_barrier((projected + proj_bias).astype(jnp.bfloat16)).astype(jnp.float32)
    padded = jnp.pad(projected, ((KS - 1, 0), (0, 0), (0, 0)))
    streams = short_bias + short_taps[0] * padded[KS - 1:]
    for offset in range(1, KS):
        streams = streams + short_taps[offset] * padded[KS - 1 - offset:KS - 1 - offset + length]
    streams = lax.optimization_barrier(streams.astype(jnp.bfloat16)).astype(jnp.float32)
    gate_out = streams[:, 0]
    mixed_in = lax.optimization_barrier((streams[:, 1] * streams[:, 2]).astype(jnp.bfloat16)).astype(jnp.float32)
    tm_count = N_TM
    digits = tm_count.bit_length() - 1
    spectral_rows = jnp.arange(2 * tm_count, dtype=jnp.int32)
    owner_row = reverse_bits(spectral_rows // 2, digits)
    parity = spectral_rows % 2
    ordered = spectrum[:, owner_row, parity]
    natural = ordered.transpose(0, 2, 1, 3).reshape(2, FFT, D)
    groups = D // 64
    signal_blocks = mixed_in.reshape(length, groups, 64).transpose(1, 0, 2)
    filter_blocks = natural.reshape(2, FFT, groups, 64).transpose(2, 0, 1, 3)

    def convolve(operands):
        signal, response = operands
        padded_sig = jnp.concatenate([signal, jnp.zeros_like(signal)], 0)
        spectral = jnp.fft.fft(padded_sig, axis=0)
        product = (response[0] + 1j * response[1]) * spectral
        return jnp.real(jnp.fft.ifft(product, axis=0))[:length]

    convolved = lax.map(convolve, (signal_blocks, filter_blocks)).transpose(1, 0, 2).reshape(length, D)
    gated_rows = ((convolved + skip_gain * mixed_in) * gate_out).astype(jnp.bfloat16)
    mixed_out = jnp.dot(gated_rows, out_weight, preferred_element_type=jnp.float32) + out_bias
    return mixed_out.astype(jnp.bfloat16)
```

```python
import math

import jax
import jax.numpy as jnp
import numpy as np
from jax import lax
from jax.sharding import PartitionSpec as P

HI = lax.Precision.HIGHEST


def from_behind(array, axis, by):
    length = lax.axis_size(axis)
    pairs = [(i, i + by) for i in range(length) if 0 <= i + by < length]
    return lax.ppermute(array, axis, pairs)


def reverse_bits_np(values, digits):
    result = np.zeros_like(values)
    for bit_level in range(digits):
        result = result | (((values >> bit_level) & 1) << (digits - 1 - bit_level))
    return result


def dft_tables(tm_count, steps_dev):
    rows = 2 * tm_count
    digits = tm_count.bit_length() - 1
    r = np.arange(rows)
    k1 = 2 * reverse_bits_np(r // 2, digits) + (r % 2)
    m = np.arange(tm_count)
    t = np.arange(steps_dev)
    b = np.arange(steps_dev)
    period = rows * steps_dev
    ang1 = 2 * np.pi * ((k1[:, None] * m[None, :]) % rows) / rows
    ang2 = 2 * np.pi * ((t[:, None] * b[None, :]) % steps_dev) / steps_dev
    angt = 2 * np.pi * ((k1[:, None] * t[None, :]) % period) / period
    f32 = lambda a: jnp.asarray(a.astype(np.float32))
    return dict(
        c1=f32(np.cos(ang1)), s1=f32(np.sin(ang1)),
        c2=f32(np.cos(ang2)), s2=f32(np.sin(ang2)),
        ct=f32(np.cos(angt)), st=f32(np.sin(angt)),
        period=period,
    )


def mm(a, b):
    return jnp.dot(a, b, precision=HI, preferred_element_type=jnp.float32)


def long_conv(x, h, tab):
    c1, s1, c2, s2, ct, st = (tab[k] for k in ("c1", "s1", "c2", "s2", "ct", "st"))
    ar = mm(c1, x)
    ai = -mm(s1, x)
    tr = ar * ct + ai * st
    ti = ai * ct - ar * st
    zr = mm(tr, c2) + mm(ti, s2)
    zi = mm(ti, c2) - mm(tr, s2)
    yr = h[0] * zr - h[1] * zi
    yi = h[0] * zi + h[1] * zr
    br = mm(yr, c2) - mm(yi, s2)
    bi = mm(yi, c2) + mm(yr, s2)
    ur = br * ct - bi * st
    ui = bi * ct + br * st
    y = lax.dot_general(c1, ur, (((0,), (0,)), ((), ())), precision=HI,
                        preferred_element_type=jnp.float32)
    y = y - lax.dot_general(s1, ui, (((0,), (0,)), ((), ())), precision=HI,
                            preferred_element_type=jnp.float32)
    return y * (1.0 / tab["period"])


def shards(series, proj_weight, proj_bias, short_taps, short_bias, spectrum,
           skip_gain, out_weight, out_bias):
    steps_dev = series.shape[0]
    model_width = proj_weight.shape[0]
    channels = proj_weight.shape[2]
    tm_count = lax.axis_size("tm")
    tab = dft_tables(tm_count, steps_dev)

    flat_weight = proj_weight.reshape(model_width, 3 * channels)
    projected = jnp.dot(
        lax.all_gather(series, "chan", axis=1, tiled=True),
        flat_weight,
        preferred_element_type=jnp.float32,
    )
    projected = (projected.reshape(steps_dev, 3, channels) + proj_bias).astype(jnp.bfloat16)
    taps_count = short_taps.shape[0]
    earlier = from_behind(projected[steps_dev - taps_count + 1:], "tm", 1)
    extended = jnp.concatenate([earlier, projected], 0).astype(jnp.float32)
    streams = short_bias + short_taps[0] * extended[taps_count - 1:]
    for offset in range(1, taps_count):
        streams = (
            streams
            + short_taps[offset]
            * extended[taps_count - 1 - offset: taps_count - 1 - offset + steps_dev]
        )
    streams = streams.astype(jnp.bfloat16)
    gate_out = streams[:, 0]
    mixed_in = (streams[:, 1].astype(jnp.float32) * streams[:, 2].astype(jnp.float32)).astype(jnp.bfloat16)

    pair = jnp.stack([mixed_in, gate_out])[:, None]
    pair = lax.all_to_all(pair, "tm", 3, 1, tiled=True)
    signal_bf = pair[0, :, :, 0]
    gate_own = pair[1, :, :, 0].astype(jnp.float32)
    h = lax.all_to_all(spectrum, "tm", 4, 1, tiled=True)
    h = h.reshape(2, 2 * tm_count, steps_dev)

    signal = signal_bf.astype(jnp.float32)
    convolved = long_conv(signal, h, tab)
    skip = lax.dynamic_index_in_dim(skip_gain, lax.axis_index("tm"), 0, keepdims=False)
    gated = ((convolved + skip * signal) * gate_own).astype(jnp.bfloat16)

    gated = lax.all_to_all(gated[:, :, None], "tm", 0, 2, tiled=True)
    gated = lax.all_gather(gated[0], "chan", axis=1, tiled=True)
    column_start = lax.axis_index("chan") * channels
    weight_cols = lax.dynamic_slice_in_dim(out_weight, column_start, channels, 1)
    mixed_out = jnp.dot(gated, weight_cols, preferred_element_type=jnp.float32) + out_bias
    return mixed_out.astype(jnp.bfloat16)


def solution(mesh):
    return jax.shard_map(
        shards,
        mesh=mesh,
        in_specs=(
            P("tm", "chan"),
            P(None, None, "chan"),
            P(None, "chan"),
            P(None, None, "chan"),
            P(None, "chan"),
            P(None, "tm", None, None, "chan"),
            P("chan"),
            P(),
            P("chan"),
        ),
        out_specs=P("tm", "chan"),
        check_vma=False,
    )
```

```python
import math

import jax
import jax.numpy as jnp
import numpy as np
from jax import lax
from jax.sharding import PartitionSpec as P

HI = lax.Precision.HIGHEST


def from_behind(array, axis, by):
    length = lax.axis_size(axis)
    pairs = [(i, i + by) for i in range(length) if 0 <= i + by < length]
    return lax.ppermute(array, axis, pairs)


def reverse_bits_np(values, digits):
    result = np.zeros_like(values)
    for bit_level in range(digits):
        result = result | (((values >> bit_level) & 1) << (digits - 1 - bit_level))
    return result


def dft_tables(tm_count, steps_dev):
    rows = 2 * tm_count
    digits = tm_count.bit_length() - 1
    r = np.arange(rows)
    k1 = 2 * reverse_bits_np(r // 2, digits) + (r % 2)
    m = np.arange(tm_count)
    t = np.arange(steps_dev)
    b = np.arange(steps_dev)
    period = rows * steps_dev
    ang1 = 2 * np.pi * ((k1[:, None] * m[None, :]) % rows) / rows
    ang2 = 2 * np.pi * ((t[:, None] * b[None, :]) % steps_dev) / steps_dev
    angt = 2 * np.pi * ((k1[:, None] * t[None, :]) % period) / period
    f32 = lambda a: jnp.asarray(a.astype(np.float32))
    return dict(
        c1=f32(np.cos(ang1)), s1=f32(np.sin(ang1)),
        c2=f32(np.cos(ang2)), s2=f32(np.sin(ang2)),
        ct=f32(np.cos(angt)), st=f32(np.sin(angt)),
        period=period,
    )


def mm(a, b):
    return jnp.dot(a, b, precision=HI, preferred_element_type=jnp.float32)


def long_conv(x, h, tab):
    c1, s1, c2, s2, ct, st = (tab[k] for k in ("c1", "s1", "c2", "s2", "ct", "st"))
    ar = mm(c1, x)
    ai = -mm(s1, x)
    tr = ar * ct + ai * st
    ti = ai * ct - ar * st
    zr = mm(tr, c2) + mm(ti, s2)
    zi = mm(ti, c2) - mm(tr, s2)
    yr = h[0] * zr - h[1] * zi
    yi = h[0] * zi + h[1] * zr
    br = mm(yr, c2) - mm(yi, s2)
    bi = mm(yi, c2) + mm(yr, s2)
    ur = br * ct - bi * st
    ui = bi * ct + br * st
    y = lax.dot_general(c1, ur, (((0,), (0,)), ((), ())), precision=HI,
                        preferred_element_type=jnp.float32)
    y = y - lax.dot_general(s1, ui, (((0,), (0,)), ((), ())), precision=HI,
                            preferred_element_type=jnp.float32)
    return y * (1.0 / tab["period"])


def shards(series, proj_weight, proj_bias, short_taps, short_bias, spectrum,
           skip_gain, out_weight, out_bias):
    steps_dev = series.shape[0]
    model_width = proj_weight.shape[0]
    channels = proj_weight.shape[2]
    tm_count = lax.axis_size("tm")
    tab = dft_tables(tm_count, steps_dev)

    flat_weight = proj_weight.reshape(model_width, 3 * channels)
    projected = jnp.dot(
        lax.all_gather(series, "chan", axis=1, tiled=True),
        flat_weight,
        preferred_element_type=jnp.float32,
    )
    projected = (projected.reshape(steps_dev, 3, channels) + proj_bias).astype(jnp.bfloat16)
    taps_count = short_taps.shape[0]
    earlier = from_behind(projected[steps_dev - taps_count + 1:], "tm", 1)
    extended = jnp.concatenate([earlier, projected], 0).astype(jnp.float32)
    streams = short_bias + short_taps[0] * extended[taps_count - 1:]
    for offset in range(1, taps_count):
        streams = (
            streams
            + short_taps[offset]
            * extended[taps_count - 1 - offset: taps_count - 1 - offset + steps_dev]
        )
    streams = streams.astype(jnp.bfloat16)
    gate_out = streams[:, 0]
    mixed_in = (streams[:, 1].astype(jnp.float32) * streams[:, 2].astype(jnp.float32)).astype(jnp.bfloat16)

    send = jnp.concatenate(
        [spectrum.reshape(-1, channels), mixed_in.astype(jnp.float32), gate_out.astype(jnp.float32)], 0)
    recv = lax.all_to_all(send[None], "tm", 2, 0, tiled=True)[:, :, 0]
    spec_len = spectrum.size // channels
    h = recv[:, :spec_len].reshape(tm_count, 2, spec_len // 2)
    h = jnp.stack([h[:, 0].reshape(2 * tm_count, steps_dev), h[:, 1].reshape(2 * tm_count, steps_dev)])
    signal_bf = recv[:, spec_len:spec_len + steps_dev]
    gate_own = recv[:, spec_len + steps_dev:]

    signal = signal_bf.astype(jnp.float32)
    convolved = long_conv(signal, h, tab)
    skip = lax.dynamic_index_in_dim(skip_gain, lax.axis_index("tm"), 0, keepdims=False)
    gated = ((convolved + skip * signal) * gate_own).astype(jnp.bfloat16)

    gated = lax.all_to_all(gated[:, :, None], "tm", 0, 2, tiled=True)
    gated = lax.all_gather(gated[0], "chan", axis=1, tiled=True)
    column_start = lax.axis_index("chan") * channels
    weight_cols = lax.dynamic_slice_in_dim(out_weight, column_start, channels, 1)
    mixed_out = jnp.dot(gated, weight_cols, preferred_element_type=jnp.float32) + out_bias
    return mixed_out.astype(jnp.bfloat16)


def solution(mesh):
    return jax.shard_map(
        shards,
        mesh=mesh,
        in_specs=(
            P("tm", "chan"),
            P(None, None, "chan"),
            P(None, "chan"),
            P(None, None, "chan"),
            P(None, "chan"),
            P(None, "tm", None, None, "chan"),
            P("chan"),
            P(),
            P("chan"),
        ),
        out_specs=P("tm", "chan"),
        check_vma=False,
    )
```

```python
import math

import jax
import jax.numpy as jnp
import numpy as np
from jax import lax
from jax.sharding import PartitionSpec as P

HI = lax.Precision.HIGHEST


def from_behind(array, axis, by):
    length = lax.axis_size(axis)
    pairs = [(i, i + by) for i in range(length) if 0 <= i + by < length]
    return lax.ppermute(array, axis, pairs)


def reverse_bits_np(values, digits):
    result = np.zeros_like(values)
    for bit_level in range(digits):
        result = result | (((values >> bit_level) & 1) << (digits - 1 - bit_level))
    return result


def dft_tables(tm_count, steps_dev):
    rows = 2 * tm_count
    digits = tm_count.bit_length() - 1
    r = np.arange(rows)
    k1 = 2 * reverse_bits_np(r // 2, digits) + (r % 2)
    m = np.arange(tm_count)
    t = np.arange(steps_dev)
    b = np.arange(steps_dev)
    period = rows * steps_dev
    ang1 = 2 * np.pi * ((k1[:, None] * m[None, :]) % rows) / rows
    ang2 = 2 * np.pi * ((t[:, None] * b[None, :]) % steps_dev) / steps_dev
    angt = 2 * np.pi * ((k1[:, None] * t[None, :]) % period) / period
    f32 = lambda a: jnp.asarray(a.astype(np.float32))
    return dict(
        c1=f32(np.cos(ang1)), s1=f32(np.sin(ang1)),
        c2=f32(np.cos(ang2)), s2=f32(np.sin(ang2)),
        ct=f32(np.cos(angt)), st=f32(np.sin(angt)),
        period=period,
    )


def mm(a, b):
    return jnp.dot(a, b, precision=HI, preferred_element_type=jnp.float32)


def long_conv(x, h, tab):
    c1, s1, c2, s2, ct, st = (tab[k] for k in ("c1", "s1", "c2", "s2", "ct", "st"))
    ar = mm(c1, x)
    ai = -mm(s1, x)
    tr = ar * ct + ai * st
    ti = ai * ct - ar * st
    zr = mm(tr, c2) + mm(ti, s2)
    zi = mm(ti, c2) - mm(tr, s2)
    yr = h[0] * zr - h[1] * zi
    yi = h[0] * zi + h[1] * zr
    br = mm(yr, c2) - mm(yi, s2)
    bi = mm(yi, c2) + mm(yr, s2)
    ur = br * ct - bi * st
    ui = bi * ct + br * st
    y = lax.dot_general(c1, ur, (((0,), (0,)), ((), ())), precision=HI,
                        preferred_element_type=jnp.float32)
    y = y - lax.dot_general(s1, ui, (((0,), (0,)), ((), ())), precision=HI,
                            preferred_element_type=jnp.float32)
    return y * (1.0 / tab["period"])


def shards(series, proj_weight, proj_bias, short_taps, short_bias, spectrum,
           skip_gain, out_weight, out_bias):
    steps_dev = series.shape[0]
    model_width = proj_weight.shape[0]
    channels = proj_weight.shape[2]
    tm_count = lax.axis_size("tm")
    tab = dft_tables(tm_count, steps_dev)

    flat_weight = proj_weight.reshape(model_width, 3 * channels)
    projected = jnp.dot(
        lax.all_gather(series, "chan", axis=1, tiled=True),
        flat_weight,
        preferred_element_type=jnp.float32,
    )
    projected = lax.reduce_precision(projected.reshape(steps_dev, 3, channels) + proj_bias, 8, 7)
    projected = projected.astype(jnp.bfloat16)
    taps_count = short_taps.shape[0]
    earlier = from_behind(projected[steps_dev - taps_count + 1:], "tm", 1)
    extended = jnp.concatenate([earlier, projected], 0).astype(jnp.float32)
    streams = short_bias + short_taps[0] * extended[taps_count - 1:]
    for offset in range(1, taps_count):
        streams = (
            streams
            + short_taps[offset]
            * extended[taps_count - 1 - offset: taps_count - 1 - offset + steps_dev]
        )
    streams = lax.reduce_precision(streams, 8, 7)
    gate_out = streams[:, 0].astype(jnp.bfloat16)
    mixed_in = (streams[:, 1] * streams[:, 2]).astype(jnp.bfloat16)

    send = jnp.concatenate(
        [spectrum.reshape(-1, channels).astype(jnp.bfloat16), mixed_in, gate_out], 0)
    recv = lax.all_to_all(send[None], "tm", 2, 0, tiled=True)[:, :, 0]
    spec_len = spectrum.size // channels
    h = recv[:, :spec_len].astype(jnp.float32).reshape(tm_count, 2, spec_len // 2)
    h = jnp.stack([h[:, 0].reshape(2 * tm_count, steps_dev), h[:, 1].reshape(2 * tm_count, steps_dev)])
    signal_bf = recv[:, spec_len:spec_len + steps_dev]
    gate_own = recv[:, spec_len + steps_dev:].astype(jnp.float32)

    signal = signal_bf.astype(jnp.float32)
    convolved = long_conv(signal, h, tab)
    skip = lax.dynamic_index_in_dim(skip_gain, lax.axis_index("tm"), 0, keepdims=False)
    gated = ((convolved + skip * signal) * gate_own).astype(jnp.bfloat16)

    gated = lax.all_to_all(gated[:, :, None], "tm", 0, 2, tiled=True)
    gated = lax.all_gather(gated[0], "chan", axis=1, tiled=True)
    column_start = lax.axis_index("chan") * channels
    weight_cols = lax.dynamic_slice_in_dim(out_weight, column_start, channels, 1)
    mixed_out = jnp.dot(gated, weight_cols, preferred_element_type=jnp.float32) + out_bias
    return mixed_out.astype(jnp.bfloat16)


def solution(mesh):
    return jax.shard_map(
        shards,
        mesh=mesh,
        in_specs=(
            P("tm", "chan"),
            P(None, None, "chan"),
            P(None, "chan"),
            P(None, None, "chan"),
            P(None, "chan"),
            P(None, "tm", None, None, "chan"),
            P("chan"),
            P(),
            P("chan"),
        ),
        out_specs=P("tm", "chan"),
        check_vma=False,
    )
```

```python
import math

import jax
import jax.numpy as jnp
import numpy as np
from jax import lax
from jax.sharding import PartitionSpec as P

HI = lax.Precision.HIGHEST


def from_behind(array, axis, by):
    length = lax.axis_size(axis)
    pairs = [(i, i + by) for i in range(length) if 0 <= i + by < length]
    return lax.ppermute(array, axis, pairs)


def reverse_bits_np(values, digits):
    result = np.zeros_like(values)
    for bit_level in range(digits):
        result = result | (((values >> bit_level) & 1) << (digits - 1 - bit_level))
    return result


def dft_tables(tm_count, steps_dev):
    rows = 2 * tm_count
    digits = tm_count.bit_length() - 1
    r = np.arange(rows)
    k1 = 2 * reverse_bits_np(r // 2, digits) + (r % 2)
    m = np.arange(tm_count)
    t = np.arange(steps_dev)
    b = np.arange(steps_dev)
    period = rows * steps_dev
    ang1 = 2 * np.pi * ((k1[:, None] * m[None, :]) % rows) / rows
    ang2 = 2 * np.pi * ((t[:, None] * b[None, :]) % steps_dev) / steps_dev
    angt = 2 * np.pi * ((k1[:, None] * t[None, :]) % period) / period
    f32 = lambda a: jnp.asarray(a.astype(np.float32))
    return dict(
        c1=f32(np.cos(ang1)), s1=f32(np.sin(ang1)),
        c2=f32(np.cos(ang2)), s2=f32(np.sin(ang2)),
        ct=f32(np.cos(angt)), st=f32(np.sin(angt)),
        period=period,
    )


def gather_chan(x):
    count = lax.axis_size("chan")
    wide = jnp.broadcast_to(x[:, None, :], (x.shape[0], count, x.shape[1]))
    return lax.all_to_all(wide, "chan", 1, 1, tiled=True).reshape(x.shape[0], count * x.shape[1])


def mm(a, b):
    return jnp.dot(a, b, precision=HI, preferred_element_type=jnp.float32)


def long_conv(x, h, tab):
    c1, s1, c2, s2, ct, st = (tab[k] for k in ("c1", "s1", "c2", "s2", "ct", "st"))
    ar = mm(c1, x)
    ai = -mm(s1, x)
    tr = ar * ct + ai * st
    ti = ai * ct - ar * st
    zr = mm(tr, c2) + mm(ti, s2)
    zi = mm(ti, c2) - mm(tr, s2)
    yr = h[0] * zr - h[1] * zi
    yi = h[0] * zi + h[1] * zr
    br = mm(yr, c2) - mm(yi, s2)
    bi = mm(yi, c2) + mm(yr, s2)
    ur = br * ct - bi * st
    ui = bi * ct + br * st
    y = lax.dot_general(c1, ur, (((0,), (0,)), ((), ())), precision=HI,
                        preferred_element_type=jnp.float32)
    y = y - lax.dot_general(s1, ui, (((0,), (0,)), ((), ())), precision=HI,
                            preferred_element_type=jnp.float32)
    return y * (1.0 / tab["period"])


def shards(series, proj_weight, proj_bias, short_taps, short_bias, spectrum,
           skip_gain, out_weight, out_bias):
    steps_dev = series.shape[0]
    model_width = proj_weight.shape[0]
    channels = proj_weight.shape[2]
    tm_count = lax.axis_size("tm")
    tab = dft_tables(tm_count, steps_dev)

    flat_weight = proj_weight.reshape(model_width, 3 * channels)
    taps_count = short_taps.shape[0]
    halo = taps_count - 1
    rows = gather_chan(series)
    earlier = from_behind(rows[steps_dev - halo:], "tm", 1)
    projected = jnp.concatenate([
        jnp.dot(earlier, flat_weight, preferred_element_type=jnp.float32),
        jnp.dot(rows, flat_weight, preferred_element_type=jnp.float32)], 0)
    projected = lax.reduce_precision(projected.reshape(steps_dev + halo, 3, channels) + proj_bias, 8, 7)
    first = lax.axis_index("tm") == 0
    keep = jnp.logical_not(first) | (jnp.arange(steps_dev + halo) >= halo)
    extended = jnp.where(keep[:, None, None], projected, 0.0)
    streams = short_bias + short_taps[0] * extended[taps_count - 1:]
    for offset in range(1, taps_count):
        streams = (
            streams
            + short_taps[offset]
            * extended[taps_count - 1 - offset: taps_count - 1 - offset + steps_dev]
        )
    streams = lax.reduce_precision(streams, 8, 7)
    gate_out = streams[:, 0].astype(jnp.bfloat16)
    mixed_in = (streams[:, 1] * streams[:, 2]).astype(jnp.bfloat16)

    send = jnp.concatenate(
        [spectrum.reshape(-1, channels).astype(jnp.bfloat16), mixed_in, gate_out], 0)
    recv = lax.all_to_all(send[None], "tm", 2, 0, tiled=True)[:, :, 0]
    spec_len = spectrum.size // channels
    h = recv[:, :spec_len].astype(jnp.float32).reshape(tm_count, 2, spec_len // 2)
    h = jnp.stack([h[:, 0].reshape(2 * tm_count, steps_dev), h[:, 1].reshape(2 * tm_count, steps_dev)])
    signal_bf = recv[:, spec_len:spec_len + steps_dev]
    gate_own = recv[:, spec_len + steps_dev:].astype(jnp.float32)

    signal = signal_bf.astype(jnp.float32)
    convolved = long_conv(signal, h, tab)
    skip = lax.dynamic_index_in_dim(skip_gain, lax.axis_index("tm"), 0, keepdims=False)
    gated = ((convolved + skip * signal) * gate_own).astype(jnp.bfloat16)

    gated = lax.all_to_all(gated[:, :, None], "tm", 0, 2, tiled=True)
    gated = gather_chan(gated[0])
    column_start = lax.axis_index("chan") * channels
    weight_cols = lax.dynamic_slice_in_dim(out_weight, column_start, channels, 1)
    mixed_out = jnp.dot(gated, weight_cols, preferred_element_type=jnp.float32) + out_bias
    return mixed_out.astype(jnp.bfloat16)


def solution(mesh):
    return jax.shard_map(
        shards,
        mesh=mesh,
        in_specs=(
            P("tm", "chan"),
            P(None, None, "chan"),
            P(None, "chan"),
            P(None, None, "chan"),
            P(None, "chan"),
            P(None, "tm", None, None, "chan"),
            P("chan"),
            P(),
            P("chan"),
        ),
        out_specs=P("tm", "chan"),
        check_vma=False,
    )
```

```python
import jax
import jax.numpy as jnp
import numpy as np
from jax import lax
from jax.sharding import PartitionSpec as P


HI = lax.Precision.HIGHEST


def from_behind(array, axis, by):
    length = lax.axis_size(axis)
    pairs = [(i, i + by) for i in range(length) if 0 <= i + by < length]
    return lax.ppermute(array, axis, pairs)


def reverse_bits_np(values, digits):
    result = np.zeros_like(values)
    for bit_level in range(digits):
        result = result | (((values >> bit_level) & 1) << (digits - 1 - bit_level))
    return result


def dft_tables(tm_count, steps_dev):
    rows = 2 * tm_count
    digits = tm_count.bit_length() - 1
    r = np.arange(rows)
    k1 = 2 * reverse_bits_np(r // 2, digits) + (r % 2)
    m = np.arange(tm_count)
    t = np.arange(steps_dev)
    b = np.arange(steps_dev)
    period = rows * steps_dev
    ang1 = 2 * np.pi * ((k1[:, None] * m[None, :]) % rows) / rows
    ang2 = 2 * np.pi * ((t[:, None] * b[None, :]) % steps_dev) / steps_dev
    angt = 2 * np.pi * ((k1[:, None] * t[None, :]) % period) / period
    f32 = lambda a: jnp.asarray(a.astype(np.float32))
    return dict(
        c1=f32(np.cos(ang1)), s1=f32(np.sin(ang1)),
        c2=f32(np.cos(ang2)), s2=f32(np.sin(ang2)),
        ct=f32(np.cos(angt)), st=f32(np.sin(angt)),
        period=period,
    )


def gather_chan(x):
    count = lax.axis_size("chan")
    wide = jnp.broadcast_to(x[:, None, :], (x.shape[0], count, x.shape[1]))
    return lax.all_to_all(wide, "chan", 1, 1, tiled=True).reshape(x.shape[0], count * x.shape[1])


def mm(a, b):
    return jnp.dot(a, b, precision=HI, preferred_element_type=jnp.float32)


def long_conv(x, h, tab):
    c1, s1, c2, s2, ct, st = (tab[k] for k in ("c1", "s1", "c2", "s2", "ct", "st"))
    ar = mm(c1, x)
    ai = -mm(s1, x)
    tr = ar * ct + ai * st
    ti = ai * ct - ar * st
    zr = mm(tr, c2) + mm(ti, s2)
    zi = mm(ti, c2) - mm(tr, s2)
    yr = h[0] * zr - h[1] * zi
    yi = h[0] * zi + h[1] * zr
    br = mm(yr, c2) - mm(yi, s2)
    bi = mm(yi, c2) + mm(yr, s2)
    ur = br * ct - bi * st
    ui = bi * ct + br * st
    y = lax.dot_general(c1, ur, (((0,), (0,)), ((), ())), precision=HI,
                        preferred_element_type=jnp.float32)
    y = y - lax.dot_general(s1, ui, (((0,), (0,)), ((), ())), precision=HI,
                            preferred_element_type=jnp.float32)
    return y * (1.0 / tab["period"])


def shards(series, proj_weight, proj_bias, short_taps, short_bias, spectrum,
           skip_gain, out_weight, out_bias):
    steps_dev = series.shape[0]
    model_width = proj_weight.shape[0]
    channels = proj_weight.shape[2]
    tm_count = lax.axis_size("tm")
    tab = dft_tables(tm_count, steps_dev)

    flat_weight = proj_weight.reshape(model_width, 3 * channels)
    taps_count = short_taps.shape[0]
    halo = taps_count - 1
    h_recv = lax.all_to_all(spectrum.reshape(1, -1, channels).astype(jnp.bfloat16), "tm", 2, 0, tiled=True)
    rows = lax.all_gather(series, "chan", axis=1, tiled=True)
    earlier = from_behind(rows[steps_dev - halo:], "tm", 1)
    projected = jnp.concatenate([
        jnp.dot(earlier, flat_weight, preferred_element_type=jnp.float32),
        jnp.dot(rows, flat_weight, preferred_element_type=jnp.float32)], 0)
    projected = lax.reduce_precision(projected.reshape(steps_dev + halo, 3, channels) + proj_bias, 8, 7)
    first = lax.axis_index("tm") == 0
    keep = jnp.logical_not(first) | (jnp.arange(steps_dev + halo) >= halo)
    extended = jnp.where(keep[:, None, None], projected, 0.0)
    streams = short_bias + short_taps[0] * extended[taps_count - 1:]
    for offset in range(1, taps_count):
        streams = (
            streams
            + short_taps[offset]
            * extended[taps_count - 1 - offset: taps_count - 1 - offset + steps_dev]
        )
    streams = lax.reduce_precision(streams, 8, 7)
    gate_out = streams[:, 0].astype(jnp.bfloat16)
    mixed_in = (streams[:, 1] * streams[:, 2]).astype(jnp.bfloat16)

    send = jnp.concatenate([mixed_in, gate_out], 0)
    h_recv, send = lax.optimization_barrier((h_recv, send))
    recv = lax.all_to_all(send[None], "tm", 2, 0, tiled=True)[:, :, 0]
    spec_len = spectrum.size // channels
    h = h_recv[:, :, 0].astype(jnp.float32).reshape(tm_count, 2, spec_len // 2)
    h = jnp.stack([h[:, 0].reshape(2 * tm_count, steps_dev), h[:, 1].reshape(2 * tm_count, steps_dev)])
    signal_bf = recv[:, :steps_dev]
    gate_own = recv[:, steps_dev:].astype(jnp.float32)

    signal = signal_bf.astype(jnp.float32)
    convolved = long_conv(signal, h, tab)
    skip = lax.dynamic_index_in_dim(skip_gain, lax.axis_index("tm"), 0, keepdims=False)
    gated = ((convolved + skip * signal) * gate_own).astype(jnp.bfloat16)

    gated = lax.all_to_all(gated[:, :, None], "tm", 0, 2, tiled=True)
    gated = gather_chan(gated[0])
    column_start = lax.axis_index("chan") * channels
    weight_cols = lax.dynamic_slice_in_dim(out_weight, column_start, channels, 1)
    mixed_out = jnp.dot(gated, weight_cols, preferred_element_type=jnp.float32) + out_bias
    return mixed_out.astype(jnp.bfloat16)


def solution(mesh):
    return jax.shard_map(
        shards,
        mesh=mesh,
        in_specs=(
            P("tm", "chan"),
            P(None, None, "chan"),
            P(None, "chan"),
            P(None, None, "chan"),
            P(None, "chan"),
            P(None, "tm", None, None, "chan"),
            P("chan"),
            P(),
            P("chan"),
        ),
        out_specs=P("tm", "chan"),
        check_vma=False,
    )
```

```python
import math

import jax
import jax.numpy as jnp
import numpy as np
from jax import lax
from jax.sharding import PartitionSpec as P

HI = lax.Precision.HIGHEST


def from_behind(array, axis, by):
    length = lax.axis_size(axis)
    pairs = [(i, i + by) for i in range(length) if 0 <= i + by < length]
    return lax.ppermute(array, axis, pairs)


def reverse_bits_np(values, digits):
    result = np.zeros_like(values)
    for bit_level in range(digits):
        result = result | (((values >> bit_level) & 1) << (digits - 1 - bit_level))
    return result


def dft_tables(tm_count, steps_dev):
    rows = 2 * tm_count
    digits = tm_count.bit_length() - 1
    r = np.arange(rows)
    k1 = 2 * reverse_bits_np(r // 2, digits) + (r % 2)
    m = np.arange(tm_count)
    t = np.arange(steps_dev)
    b = np.arange(steps_dev)
    period = rows * steps_dev
    ang1 = 2 * np.pi * ((k1[:, None] * m[None, :]) % rows) / rows
    ang2 = 2 * np.pi * ((t[:, None] * b[None, :]) % steps_dev) / steps_dev
    angt = 2 * np.pi * ((k1[:, None] * t[None, :]) % period) / period
    f32 = lambda a: jnp.asarray(a.astype(np.float32))
    return dict(
        c1=f32(np.cos(ang1)), s1=f32(np.sin(ang1)),
        c2=f32(np.cos(ang2)), s2=f32(np.sin(ang2)),
        ct=f32(np.cos(angt)), st=f32(np.sin(angt)),
        period=period,
    )


def gather_chan(x):
    count = lax.axis_size("chan")
    wide = jnp.broadcast_to(x[:, None, :], (x.shape[0], count, x.shape[1]))
    return lax.all_to_all(wide, "chan", 1, 1, tiled=True).reshape(x.shape[0], count * x.shape[1])


def mm(a, b):
    return jnp.dot(a, b, precision=HI, preferred_element_type=jnp.float32)


def long_conv(x, h, tab):
    c1, s1, c2, s2, ct, st = (tab[k] for k in ("c1", "s1", "c2", "s2", "ct", "st"))
    ar = mm(c1, x)
    ai = -mm(s1, x)
    tr = ar * ct + ai * st
    ti = ai * ct - ar * st
    zr = mm(tr, c2) + mm(ti, s2)
    zi = mm(ti, c2) - mm(tr, s2)
    yr = h[0] * zr - h[1] * zi
    yi = h[0] * zi + h[1] * zr
    br = mm(yr, c2) - mm(yi, s2)
    bi = mm(yi, c2) + mm(yr, s2)
    ur = br * ct - bi * st
    ui = bi * ct + br * st
    y = lax.dot_general(c1, ur, (((0,), (0,)), ((), ())), precision=HI,
                        preferred_element_type=jnp.float32)
    y = y - lax.dot_general(s1, ui, (((0,), (0,)), ((), ())), precision=HI,
                            preferred_element_type=jnp.float32)
    return y * (1.0 / tab["period"])


def shards(series, proj_weight, proj_bias, short_taps, short_bias, spectrum,
           skip_gain, out_weight, out_bias):
    steps_dev = series.shape[0]
    model_width = proj_weight.shape[0]
    channels = proj_weight.shape[2]
    tm_count = lax.axis_size("tm")
    tab = dft_tables(tm_count, steps_dev)

    flat_weight = proj_weight.reshape(model_width, 3 * channels)
    taps_count = short_taps.shape[0]
    halo = taps_count - 1
    rows = gather_chan(series)
    earlier = from_behind(rows[steps_dev - halo:], "tm", 1)
    projected = jnp.concatenate([
        jnp.dot(earlier, flat_weight, preferred_element_type=jnp.float32),
        jnp.dot(rows, flat_weight, preferred_element_type=jnp.float32)], 0)
    projected = lax.reduce_precision(projected.reshape(steps_dev + halo, 3, channels) + proj_bias, 8, 7)
    first = lax.axis_index("tm") == 0
    keep = jnp.logical_not(first) | (jnp.arange(steps_dev + halo) >= halo)
    extended = jnp.where(keep[:, None, None], projected, 0.0)
    streams = short_bias + short_taps[0] * extended[taps_count - 1:]
    for offset in range(1, taps_count):
        streams = (
            streams
            + short_taps[offset]
            * extended[taps_count - 1 - offset: taps_count - 1 - offset + steps_dev]
        )
    streams = lax.reduce_precision(streams, 8, 7)
    gate_out = streams[:, 0].astype(jnp.bfloat16)
    mixed_in = (streams[:, 1] * streams[:, 2]).astype(jnp.bfloat16)

    send = jnp.concatenate(
        [spectrum.reshape(-1, channels).astype(jnp.bfloat16), mixed_in, gate_out], 0)
    recv = lax.all_to_all(send.T, "tm", 0, 0, tiled=True)
    spec_len = spectrum.size // channels
    h = recv[:, :spec_len].astype(jnp.float32).reshape(tm_count, 2, spec_len // 2)
    h = jnp.stack([h[:, 0].reshape(2 * tm_count, steps_dev), h[:, 1].reshape(2 * tm_count, steps_dev)])
    signal_bf = recv[:, spec_len:spec_len + steps_dev]
    gate_own = recv[:, spec_len + steps_dev:].astype(jnp.float32)

    signal = signal_bf.astype(jnp.float32)
    convolved = long_conv(signal, h, tab)
    skip = lax.dynamic_index_in_dim(skip_gain, lax.axis_index("tm"), 0, keepdims=False)
    gated = ((convolved + skip * signal) * gate_own).astype(jnp.bfloat16)

    gated = lax.all_to_all(gated, "tm", 0, 0, tiled=True).T
    gated = gather_chan(gated)
    column_start = lax.axis_index("chan") * channels
    weight_cols = lax.dynamic_slice_in_dim(out_weight, column_start, channels, 1)
    mixed_out = jnp.dot(gated, weight_cols, preferred_element_type=jnp.float32) + out_bias
    return mixed_out.astype(jnp.bfloat16)


def solution(mesh):
    return jax.shard_map(
        shards,
        mesh=mesh,
        in_specs=(
            P("tm", "chan"),
            P(None, None, "chan"),
            P(None, "chan"),
            P(None, None, "chan"),
            P(None, "chan"),
            P(None, "tm", None, None, "chan"),
            P("chan"),
            P(),
            P("chan"),
        ),
        out_specs=P("tm", "chan"),
        check_vma=False,
    )
```

```python
import math

import jax
import jax.numpy as jnp
import numpy as np
from jax import lax
from jax.sharding import PartitionSpec as P

HI = lax.Precision.HIGH


def from_behind(array, axis, by):
    length = lax.axis_size(axis)
    pairs = [(i, i + by) for i in range(length) if 0 <= i + by < length]
    return lax.ppermute(array, axis, pairs)


def reverse_bits_np(values, digits):
    result = np.zeros_like(values)
    for bit_level in range(digits):
        result = result | (((values >> bit_level) & 1) << (digits - 1 - bit_level))
    return result


def dft_tables(tm_count, steps_dev):
    rows = 2 * tm_count
    digits = tm_count.bit_length() - 1
    r = np.arange(rows)
    k1 = 2 * reverse_bits_np(r // 2, digits) + (r % 2)
    m = np.arange(tm_count)
    t = np.arange(steps_dev)
    b = np.arange(steps_dev)
    period = rows * steps_dev
    ang1 = 2 * np.pi * ((k1[:, None] * m[None, :]) % rows) / rows
    ang2 = 2 * np.pi * ((t[:, None] * b[None, :]) % steps_dev) / steps_dev
    angt = 2 * np.pi * ((k1[:, None] * t[None, :]) % period) / period
    f32 = lambda a: jnp.asarray(a.astype(np.float32))
    return dict(
        c1=f32(np.cos(ang1)), s1=f32(np.sin(ang1)),
        c2=f32(np.cos(ang2)), s2=f32(np.sin(ang2)),
        ct=f32(np.cos(angt)), st=f32(np.sin(angt)),
        period=period,
    )


def gather_chan(x):
    count = lax.axis_size("chan")
    wide = jnp.broadcast_to(x[:, None, :], (x.shape[0], count, x.shape[1]))
    return lax.all_to_all(wide, "chan", 1, 1, tiled=True).reshape(x.shape[0], count * x.shape[1])


def mm(a, b):
    return jnp.dot(a, b, precision=HI, preferred_element_type=jnp.float32)


def long_conv(x, h, tab):
    c1, s1, c2, s2, ct, st = (tab[k] for k in ("c1", "s1", "c2", "s2", "ct", "st"))
    ar = mm(c1, x)
    ai = -mm(s1, x)
    tr = ar * ct + ai * st
    ti = ai * ct - ar * st
    zr = mm(tr, c2) + mm(ti, s2)
    zi = mm(ti, c2) - mm(tr, s2)
    yr = h[0] * zr - h[1] * zi
    yi = h[0] * zi + h[1] * zr
    br = mm(yr, c2) - mm(yi, s2)
    bi = mm(yi, c2) + mm(yr, s2)
    ur = br * ct - bi * st
    ui = bi * ct + br * st
    y = lax.dot_general(c1, ur, (((0,), (0,)), ((), ())), precision=HI,
                        preferred_element_type=jnp.float32)
    y = y - lax.dot_general(s1, ui, (((0,), (0,)), ((), ())), precision=HI,
                            preferred_element_type=jnp.float32)
    return y * (1.0 / tab["period"])


def shards(series, proj_weight, proj_bias, short_taps, short_bias, spectrum,
           skip_gain, out_weight, out_bias):
    steps_dev = series.shape[0]
    model_width = proj_weight.shape[0]
    channels = proj_weight.shape[2]
    tm_count = lax.axis_size("tm")
    tab = dft_tables(tm_count, steps_dev)

    flat_weight = proj_weight.reshape(model_width, 3 * channels)
    taps_count = short_taps.shape[0]
    halo = taps_count - 1
    rows = gather_chan(series)
    earlier = from_behind(rows[steps_dev - halo:], "tm", 1)
    projected = jnp.concatenate([
        jnp.dot(earlier, flat_weight, preferred_element_type=jnp.float32),
        jnp.dot(rows, flat_weight, preferred_element_type=jnp.float32)], 0)
    projected = lax.reduce_precision(projected.reshape(steps_dev + halo, 3, channels) + proj_bias, 8, 7)
    first = lax.axis_index("tm") == 0
    keep = jnp.logical_not(first) | (jnp.arange(steps_dev + halo) >= halo)
    extended = jnp.where(keep[:, None, None], projected, 0.0)
    streams = short_bias + short_taps[0] * extended[taps_count - 1:]
    for offset in range(1, taps_count):
        streams = (
            streams
            + short_taps[offset]
            * extended[taps_count - 1 - offset: taps_count - 1 - offset + steps_dev]
        )
    streams = lax.reduce_precision(streams, 8, 7)
    gate_out = streams[:, 0].astype(jnp.bfloat16)
    mixed_in = (streams[:, 1] * streams[:, 2]).astype(jnp.bfloat16)

    send = jnp.concatenate(
        [spectrum.reshape(-1, channels).astype(jnp.bfloat16), mixed_in, gate_out], 0)
    recv = lax.all_to_all(send.T, "tm", 0, 0, tiled=True)
    spec_len = spectrum.size // channels
    h = recv[:, :spec_len].astype(jnp.float32).reshape(tm_count, 2, spec_len // 2)
    h = jnp.stack([h[:, 0].reshape(2 * tm_count, steps_dev), h[:, 1].reshape(2 * tm_count, steps_dev)])
    signal_bf = recv[:, spec_len:spec_len + steps_dev]
    gate_own = recv[:, spec_len + steps_dev:].astype(jnp.float32)

    signal = signal_bf.astype(jnp.float32)
    convolved = long_conv(signal, h, tab)
    skip = lax.dynamic_index_in_dim(skip_gain, lax.axis_index("tm"), 0, keepdims=False)
    gated = ((convolved + skip * signal) * gate_own).astype(jnp.bfloat16)

    gated = lax.all_to_all(gated, "tm", 0, 0, tiled=True).T
    gated = gather_chan(gated)
    column_start = lax.axis_index("chan") * channels
    weight_cols = lax.dynamic_slice_in_dim(out_weight, column_start, channels, 1)
    mixed_out = jnp.dot(gated, weight_cols, preferred_element_type=jnp.float32) + out_bias
    return mixed_out.astype(jnp.bfloat16)


def solution(mesh):
    return jax.shard_map(
        shards,
        mesh=mesh,
        in_specs=(
            P("tm", "chan"),
            P(None, None, "chan"),
            P(None, "chan"),
            P(None, None, "chan"),
            P(None, "chan"),
            P(None, "tm", None, None, "chan"),
            P("chan"),
            P(),
            P("chan"),
        ),
        out_specs=P("tm", "chan"),
        check_vma=False,
    )
```

```python
import math

import jax
import jax.numpy as jnp
import numpy as np
from jax import lax
from jax.sharding import PartitionSpec as P

HI = lax.Precision.HIGH


def from_behind(array, axis, by):
    length = lax.axis_size(axis)
    pairs = [(i, i + by) for i in range(length) if 0 <= i + by < length]
    return lax.ppermute(array, axis, pairs)


def reverse_bits_np(values, digits):
    result = np.zeros_like(values)
    for bit_level in range(digits):
        result = result | (((values >> bit_level) & 1) << (digits - 1 - bit_level))
    return result


def dft_tables(tm_count, steps_dev):
    rows = 2 * tm_count
    digits = tm_count.bit_length() - 1
    r = np.arange(rows)
    k1 = 2 * reverse_bits_np(r // 2, digits) + (r % 2)
    m = np.arange(tm_count)
    t = np.arange(steps_dev)
    b = np.arange(steps_dev)
    period = rows * steps_dev
    ang1 = 2 * np.pi * ((k1[:, None] * m[None, :]) % rows) / rows
    ang2 = 2 * np.pi * ((t[:, None] * b[None, :]) % steps_dev) / steps_dev
    angt = 2 * np.pi * ((k1[:, None] * t[None, :]) % period) / period
    f32 = lambda a: jnp.asarray(a.astype(np.float32))
    return dict(
        c1=f32(np.cos(ang1)), s1=f32(np.sin(ang1)),
        c2=f32(np.cos(ang2)), s2=f32(np.sin(ang2)),
        ct=f32(np.cos(angt)), st=f32(np.sin(angt)),
        period=period,
    )


def gather_chan(x):
    count = lax.axis_size("chan")
    wide = jnp.broadcast_to(x[:, None, :], (x.shape[0], count, x.shape[1]))
    return lax.all_to_all(wide, "chan", 1, 1, tiled=True).reshape(x.shape[0], count * x.shape[1])


def mm(a, b):
    return jnp.dot(a, b, precision=HI, preferred_element_type=jnp.float32)


def long_conv(x, h, tab):
    c1, s1, c2, s2, ct, st = (tab[k] for k in ("c1", "s1", "c2", "s2", "ct", "st"))
    ar = mm(c1, x)
    ai = -mm(s1, x)
    tr = ar * ct + ai * st
    ti = ai * ct - ar * st
    zr = mm(tr, c2) + mm(ti, s2)
    zi = mm(ti, c2) - mm(tr, s2)
    yr = h[0] * zr - h[1] * zi
    yi = h[0] * zi + h[1] * zr
    br = mm(yr, c2) - mm(yi, s2)
    bi = mm(yi, c2) + mm(yr, s2)
    ur = br * ct - bi * st
    ui = bi * ct + br * st
    y = lax.dot_general(c1, ur, (((0,), (0,)), ((), ())), precision=HI,
                        preferred_element_type=jnp.float32)
    y = y - lax.dot_general(s1, ui, (((0,), (0,)), ((), ())), precision=HI,
                            preferred_element_type=jnp.float32)
    return y * (1.0 / tab["period"])


def shards(series, proj_weight, proj_bias, short_taps, short_bias, spectrum,
           skip_gain, out_weight, out_bias):
    steps_dev = series.shape[0]
    model_width = proj_weight.shape[0]
    channels = proj_weight.shape[2]
    tm_count = lax.axis_size("tm")
    tab = dft_tables(tm_count, steps_dev)

    flat_weight = proj_weight.reshape(model_width, 3 * channels)
    taps_count = short_taps.shape[0]
    halo = taps_count - 1
    rows = gather_chan(series)
    projected = jnp.dot(rows, flat_weight, preferred_element_type=jnp.float32)
    projected = (projected.reshape(steps_dev, 3, channels) + proj_bias).astype(jnp.bfloat16)

    send = jnp.concatenate(
        [spectrum.reshape(-1, channels).astype(jnp.bfloat16),
         projected.transpose(1, 0, 2).reshape(3 * steps_dev, channels)], 0)
    recv = lax.all_to_all(send.T, "tm", 0, 0, tiled=True)
    spec_len = spectrum.size // channels
    h = recv[:, :spec_len].astype(jnp.float32).reshape(tm_count, 2, spec_len // 2)
    h = jnp.stack([h[:, 0].reshape(2 * tm_count, steps_dev), h[:, 1].reshape(2 * tm_count, steps_dev)])
    own = lax.axis_index("tm")
    taps = lax.dynamic_index_in_dim(short_taps, own, 2, keepdims=False)
    bias = lax.dynamic_index_in_dim(short_bias, own, 1, keepdims=False)
    length = tm_count * steps_dev
    flat = recv[:, spec_len:].reshape(tm_count, 3, steps_dev).transpose(1, 0, 2).reshape(3, length)
    flat = flat.astype(jnp.float32)
    padded = jnp.concatenate([jnp.zeros((3, halo), jnp.float32), flat], 1)
    streams = bias[:, None] + taps[0][:, None] * padded[:, halo:]
    for offset in range(1, taps_count):
        streams = streams + taps[offset][:, None] * padded[:, halo - offset: halo - offset + length]
    streams = lax.reduce_precision(streams, 8, 7)
    gate_own = streams[0].reshape(tm_count, steps_dev)
    signal = lax.reduce_precision(streams[1] * streams[2], 8, 7).reshape(tm_count, steps_dev)
    convolved = long_conv(signal, h, tab)
    skip = lax.dynamic_index_in_dim(skip_gain, lax.axis_index("tm"), 0, keepdims=False)
    gated = ((convolved + skip * signal) * gate_own).astype(jnp.bfloat16)

    gated = lax.all_to_all(gated, "tm", 0, 0, tiled=True).T
    gated = gather_chan(gated)
    column_start = lax.axis_index("chan") * channels
    weight_cols = lax.dynamic_slice_in_dim(out_weight, column_start, channels, 1)
    mixed_out = jnp.dot(gated, weight_cols, preferred_element_type=jnp.float32) + out_bias
    return mixed_out.astype(jnp.bfloat16)


def solution(mesh):
    return jax.shard_map(
        shards,
        mesh=mesh,
        in_specs=(
            P("tm", "chan"),
            P(None, None, "chan"),
            P(None, "chan"),
            P(None, None, "chan"),
            P(None, "chan"),
            P(None, "tm", None, None, "chan"),
            P("chan"),
            P(),
            P("chan"),
        ),
        out_specs=P("tm", "chan"),
        check_vma=False,
    )
```

```python
import math

import jax
import jax.numpy as jnp
import numpy as np
from jax import lax
from jax.sharding import PartitionSpec as P

HI = lax.Precision.HIGH


def from_behind(array, axis, by):
    length = lax.axis_size(axis)
    pairs = [(i, i + by) for i in range(length) if 0 <= i + by < length]
    return lax.ppermute(array, axis, pairs)


def reverse_bits(values, digits):
    result = jnp.zeros_like(values)
    for bit_level in range(digits):
        result = result | (values >> bit_level & 1) << digits - 1 - bit_level
    return result


def dft_tables(tm_count, steps_dev):
    rows = 2 * tm_count
    digits = tm_count.bit_length() - 1
    r = lax.iota(jnp.int32, rows)
    k1 = 2 * reverse_bits(r // 2, digits) + r % 2
    m = lax.iota(jnp.int32, tm_count)
    t = lax.iota(jnp.int32, steps_dev)
    period = rows * steps_dev

    def turn(index, count):
        angle = (index % count).astype(jnp.float32) * (2 * math.pi / count)
        return jnp.cos(angle), jnp.sin(angle)

    c1, s1 = turn(k1[:, None] * m[None, :], rows)
    c2, s2 = turn(t[:, None] * t[None, :], steps_dev)
    ct, st = turn(k1[:, None] * t[None, :], period)
    c1, s1, c2, s2, ct, st = lax.optimization_barrier((c1, s1, c2, s2, ct, st))
    return dict(c1=c1, s1=s1, c2=c2, s2=s2, ct=ct, st=st, period=period)


def gather_chan(x):
    count = lax.axis_size("chan")
    wide = jnp.broadcast_to(x[:, None, :], (x.shape[0], count, x.shape[1]))
    return lax.all_to_all(wide, "chan", 1, 1, tiled=True).reshape(x.shape[0], count * x.shape[1])


def mm(a, b):
    return jnp.dot(a, b, precision=HI, preferred_element_type=jnp.float32)


def long_conv(x, h, tab):
    c1, s1, c2, s2, ct, st = (tab[k] for k in ("c1", "s1", "c2", "s2", "ct", "st"))
    ar = mm(c1, x)
    ai = -mm(s1, x)
    tr = ar * ct + ai * st
    ti = ai * ct - ar * st
    zr = mm(tr, c2) + mm(ti, s2)
    zi = mm(ti, c2) - mm(tr, s2)
    yr = h[0] * zr - h[1] * zi
    yi = h[0] * zi + h[1] * zr
    br = mm(yr, c2) - mm(yi, s2)
    bi = mm(yi, c2) + mm(yr, s2)
    ur = br * ct - bi * st
    ui = bi * ct + br * st
    y = lax.dot_general(c1, ur, (((0,), (0,)), ((), ())), precision=HI,
                        preferred_element_type=jnp.float32)
    y = y - lax.dot_general(s1, ui, (((0,), (0,)), ((), ())), precision=HI,
                            preferred_element_type=jnp.float32)
    return y * (1.0 / tab["period"])


def shards(series, proj_weight, proj_bias, short_taps, short_bias, spectrum,
           skip_gain, out_weight, out_bias):
    steps_dev = series.shape[0]
    model_width = proj_weight.shape[0]
    channels = proj_weight.shape[2]
    tm_count = lax.axis_size("tm")
    tab = dft_tables(tm_count, steps_dev)

    flat_weight = proj_weight.reshape(model_width, 3 * channels)
    taps_count = short_taps.shape[0]
    halo = taps_count - 1
    rows = gather_chan(series)
    projected = jnp.dot(rows, flat_weight, preferred_element_type=jnp.float32)
    projected = (projected.reshape(steps_dev, 3, channels) + proj_bias).astype(jnp.bfloat16)

    send = jnp.concatenate(
        [spectrum.reshape(-1, channels).astype(jnp.bfloat16),
         projected.transpose(1, 0, 2).reshape(3 * steps_dev, channels)], 0)
    recv = lax.all_to_all(send.T, "tm", 0, 0, tiled=True)
    spec_len = spectrum.size // channels
    h = recv[:, :spec_len].astype(jnp.float32).reshape(tm_count, 2, spec_len // 2)
    h = jnp.stack([h[:, 0].reshape(2 * tm_count, steps_dev), h[:, 1].reshape(2 * tm_count, steps_dev)])
    own = lax.axis_index("tm")
    taps = lax.dynamic_index_in_dim(short_taps, own, 2, keepdims=False)
    bias = lax.dynamic_index_in_dim(short_bias, own, 1, keepdims=False)
    length = tm_count * steps_dev
    flat = recv[:, spec_len:].reshape(tm_count, 3, steps_dev).transpose(1, 0, 2).reshape(3, length)
    flat = flat.astype(jnp.float32)
    padded = jnp.concatenate([jnp.zeros((3, halo), jnp.float32), flat], 1)
    streams = bias[:, None] + taps[0][:, None] * padded[:, halo:]
    for offset in range(1, taps_count):
        streams = streams + taps[offset][:, None] * padded[:, halo - offset: halo - offset + length]
    streams = lax.reduce_precision(streams, 8, 7)
    gate_own = streams[0].reshape(tm_count, steps_dev)
    signal = lax.reduce_precision(streams[1] * streams[2], 8, 7).reshape(tm_count, steps_dev)
    convolved = long_conv(signal, h, tab)
    skip = lax.dynamic_index_in_dim(skip_gain, lax.axis_index("tm"), 0, keepdims=False)
    gated = ((convolved + skip * signal) * gate_own).astype(jnp.bfloat16)

    gated = lax.all_to_all(gated, "tm", 0, 0, tiled=True).T
    gated = gather_chan(gated)
    column_start = lax.axis_index("chan") * channels
    weight_cols = lax.dynamic_slice_in_dim(out_weight, column_start, channels, 1)
    mixed_out = jnp.dot(gated, weight_cols, preferred_element_type=jnp.float32) + out_bias
    return mixed_out.astype(jnp.bfloat16)


def solution(mesh):
    return jax.shard_map(
        shards,
        mesh=mesh,
        in_specs=(
            P("tm", "chan"),
            P(None, None, "chan"),
            P(None, "chan"),
            P(None, None, "chan"),
            P(None, "chan"),
            P(None, "tm", None, None, "chan"),
            P("chan"),
            P(),
            P("chan"),
        ),
        out_specs=P("tm", "chan"),
        check_vma=False,
    )
```

```python
import math

import jax
import jax.numpy as jnp
import numpy as np
from jax import lax
from jax.sharding import PartitionSpec as P

HI = lax.Precision.HIGH


def from_behind(array, axis, by):
    length = lax.axis_size(axis)
    pairs = [(i, i + by) for i in range(length) if 0 <= i + by < length]
    return lax.ppermute(array, axis, pairs)


def reverse_bits(values, digits):
    result = jnp.zeros_like(values)
    for bit_level in range(digits):
        result = result | (values >> bit_level & 1) << digits - 1 - bit_level
    return result


def dft_tables(tm_count, steps_dev):
    rows = 2 * tm_count
    digits = tm_count.bit_length() - 1
    r = lax.iota(jnp.int32, rows)
    k1 = 2 * reverse_bits(r // 2, digits) + r % 2
    m = lax.iota(jnp.int32, tm_count)
    t = lax.iota(jnp.int32, steps_dev)
    period = rows * steps_dev

    def turn(index, count):
        angle = (index % count).astype(jnp.float32) * (2 * math.pi / count)
        return jnp.cos(angle), jnp.sin(angle)

    c1, s1 = turn(k1[:, None] * m[None, :], rows)
    c2, s2 = turn(t[:, None] * t[None, :], steps_dev)
    ct, st = turn(k1[:, None] * t[None, :], period)
    c1, s1, c2, s2, ct, st = lax.optimization_barrier((c1, s1, c2, s2, ct, st))
    return dict(c1=c1, s1=s1, c2=c2, s2=s2, ct=ct, st=st, period=period)


def gather_chan(x):
    count = lax.axis_size("chan")
    wide = jnp.broadcast_to(x[:, None, :], (x.shape[0], count, x.shape[1]))
    return lax.all_to_all(wide, "chan", 1, 1, tiled=True).reshape(x.shape[0], count * x.shape[1])


def mm(a, b):
    return jnp.dot(a, b, precision=HI, preferred_element_type=jnp.float32)


def long_conv(x, h, tab):
    c1, s1, c2, s2, ct, st = (tab[k] for k in ("c1", "s1", "c2", "s2", "ct", "st"))
    ar = mm(c1, x)
    ai = -mm(s1, x)
    tr = ar * ct + ai * st
    ti = ai * ct - ar * st
    zr = mm(tr, c2) + mm(ti, s2)
    zi = mm(ti, c2) - mm(tr, s2)
    yr = h[0] * zr - h[1] * zi
    yi = h[0] * zi + h[1] * zr
    br = mm(yr, c2) - mm(yi, s2)
    bi = mm(yi, c2) + mm(yr, s2)
    ur = br * ct - bi * st
    ui = bi * ct + br * st
    y = lax.dot_general(c1, ur, (((0,), (0,)), ((), ())), precision=HI,
                        preferred_element_type=jnp.float32)
    y = y - lax.dot_general(s1, ui, (((0,), (0,)), ((), ())), precision=HI,
                            preferred_element_type=jnp.float32)
    return y * (1.0 / tab["period"])


def shards(series, proj_weight, proj_bias, short_taps, short_bias, spectrum,
           skip_gain, out_weight, out_bias):
    steps_dev = series.shape[0]
    model_width = proj_weight.shape[0]
    channels = proj_weight.shape[2]
    tm_count = lax.axis_size("tm")
    tab = dft_tables(tm_count, steps_dev)

    flat_weight = proj_weight.reshape(model_width, 3 * channels)
    taps_count = short_taps.shape[0]
    halo = taps_count - 1
    rows = gather_chan(series)
    projected = jnp.dot(rows, flat_weight, preferred_element_type=jnp.float32)
    projected = (projected.reshape(steps_dev, 3, channels) + proj_bias).astype(jnp.bfloat16)

    send = jnp.concatenate(
        [spectrum.reshape(-1, channels).astype(jnp.bfloat16),
         projected.transpose(1, 0, 2).reshape(3 * steps_dev, channels)], 0)
    send = send.T.reshape(channels, 2, -1)
    recv = lax.all_to_all(send, "tm", 0, 0, tiled=True).reshape(tm_count, -1)
    spec_len = spectrum.size // channels
    h = recv[:, :spec_len].astype(jnp.float32).reshape(tm_count, 2, spec_len // 2)
    h = jnp.stack([h[:, 0].reshape(2 * tm_count, steps_dev), h[:, 1].reshape(2 * tm_count, steps_dev)])
    own = lax.axis_index("tm")
    taps = lax.dynamic_index_in_dim(short_taps, own, 2, keepdims=False)
    bias = lax.dynamic_index_in_dim(short_bias, own, 1, keepdims=False)
    length = tm_count * steps_dev
    flat = recv[:, spec_len:].reshape(tm_count, 3, steps_dev).transpose(1, 0, 2).reshape(3, length)
    flat = flat.astype(jnp.float32)
    padded = jnp.concatenate([jnp.zeros((3, halo), jnp.float32), flat], 1)
    streams = bias[:, None] + taps[0][:, None] * padded[:, halo:]
    for offset in range(1, taps_count):
        streams = streams + taps[offset][:, None] * padded[:, halo - offset: halo - offset + length]
    streams = lax.reduce_precision(streams, 8, 7)
    gate_own = streams[0].reshape(tm_count, steps_dev)
    signal = lax.reduce_precision(streams[1] * streams[2], 8, 7).reshape(tm_count, steps_dev)
    convolved = long_conv(signal, h, tab)
    skip = lax.dynamic_index_in_dim(skip_gain, lax.axis_index("tm"), 0, keepdims=False)
    gated = ((convolved + skip * signal) * gate_own).astype(jnp.bfloat16)

    gated = lax.all_to_all(gated, "tm", 0, 0, tiled=True).T
    gated = gather_chan(gated)
    column_start = lax.axis_index("chan") * channels
    weight_cols = lax.dynamic_slice_in_dim(out_weight, column_start, channels, 1)
    mixed_out = jnp.dot(gated, weight_cols, preferred_element_type=jnp.float32) + out_bias
    return mixed_out.astype(jnp.bfloat16)


def solution(mesh):
    return jax.shard_map(
        shards,
        mesh=mesh,
        in_specs=(
            P("tm", "chan"),
            P(None, None, "chan"),
            P(None, "chan"),
            P(None, None, "chan"),
            P(None, "chan"),
            P(None, "tm", None, None, "chan"),
            P("chan"),
            P(),
            P("chan"),
        ),
        out_specs=P("tm", "chan"),
        check_vma=False,
    )
```

```python
import math

import jax
import jax.numpy as jnp
import numpy as np
from jax import lax
from jax.sharding import PartitionSpec as P

HI = lax.Precision.HIGH


def from_behind(array, axis, by):
    length = lax.axis_size(axis)
    pairs = [(i, i + by) for i in range(length) if 0 <= i + by < length]
    return lax.ppermute(array, axis, pairs)


def reverse_bits(values, digits):
    result = jnp.zeros_like(values)
    for bit_level in range(digits):
        result = result | (values >> bit_level & 1) << digits - 1 - bit_level
    return result


def dft_tables(tm_count, steps_dev):
    rows = 2 * tm_count
    digits = tm_count.bit_length() - 1
    r = lax.iota(jnp.int32, rows)
    k1 = 2 * reverse_bits(r // 2, digits) + r % 2
    m = lax.iota(jnp.int32, tm_count)
    t = lax.iota(jnp.int32, steps_dev)
    period = rows * steps_dev

    def turn(index, count):
        angle = (index % count).astype(jnp.float32) * (2 * math.pi / count)
        return jnp.cos(angle), jnp.sin(angle)

    c1, s1 = turn(k1[:, None] * m[None, :], rows)
    c2, s2 = turn(t[:, None] * t[None, :], steps_dev)
    ct, st = turn(k1[:, None] * t[None, :], period)
    c1, s1, c2, s2, ct, st = lax.optimization_barrier((c1, s1, c2, s2, ct, st))
    return dict(c1=c1, s1=s1, c2=c2, s2=s2, ct=ct, st=st, period=period)


def gather_chan(x):
    count = lax.axis_size("chan")
    wide = jnp.broadcast_to(x[:, None, :], (x.shape[0], count, x.shape[1]))
    return lax.all_to_all(wide, "chan", 1, 1, tiled=True).reshape(x.shape[0], count * x.shape[1])


def mm(a, b):
    return jnp.dot(a, b, precision=HI, preferred_element_type=jnp.float32)


def long_conv(x, h, tab):
    c1, s1, c2, s2, ct, st = (tab[k] for k in ("c1", "s1", "c2", "s2", "ct", "st"))
    ar = mm(c1, x)
    ai = -mm(s1, x)
    tr = ar * ct + ai * st
    ti = ai * ct - ar * st
    zr = mm(tr, c2) + mm(ti, s2)
    zi = mm(ti, c2) - mm(tr, s2)
    yr = h[0] * zr - h[1] * zi
    yi = h[0] * zi + h[1] * zr
    br = mm(yr, c2) - mm(yi, s2)
    bi = mm(yi, c2) + mm(yr, s2)
    ur = br * ct - bi * st
    ui = bi * ct + br * st
    y = lax.dot_general(c1, ur, (((0,), (0,)), ((), ())), precision=HI,
                        preferred_element_type=jnp.float32)
    y = y - lax.dot_general(s1, ui, (((0,), (0,)), ((), ())), precision=HI,
                            preferred_element_type=jnp.float32)
    return y * (1.0 / tab["period"])


def shards(series, proj_weight, proj_bias, short_taps, short_bias, spectrum,
           skip_gain, out_weight, out_bias):
    steps_dev = series.shape[0]
    model_width = proj_weight.shape[0]
    channels = proj_weight.shape[2]
    tm_count = lax.axis_size("tm")
    tab = dft_tables(tm_count, steps_dev)

    flat_weight = proj_weight.reshape(model_width, 3 * channels)
    taps_count = short_taps.shape[0]
    halo = taps_count - 1
    rows = gather_chan(series)
    projected = jnp.dot(rows, flat_weight, preferred_element_type=jnp.float32)
    projected = (projected.reshape(steps_dev, 3, channels) + proj_bias).astype(jnp.bfloat16)

    send = jnp.concatenate(
        [spectrum.reshape(-1, channels).astype(jnp.bfloat16),
         projected.transpose(1, 0, 2).reshape(3 * steps_dev, channels)], 0)
    send = send.T.reshape(channels, 2, -1)
    recv = lax.all_to_all(send, "tm", 0, 0, tiled=True).reshape(tm_count, -1)
    spec_len = spectrum.size // channels
    h = recv[:, :spec_len].astype(jnp.float32).reshape(tm_count, 2, spec_len // 2)
    h = jnp.stack([h[:, 0].reshape(2 * tm_count, steps_dev), h[:, 1].reshape(2 * tm_count, steps_dev)])
    own = lax.axis_index("tm")
    taps = lax.dynamic_index_in_dim(short_taps, own, 2, keepdims=False)
    bias = lax.dynamic_index_in_dim(short_bias, own, 1, keepdims=False)
    length = tm_count * steps_dev
    flat = recv[:, spec_len:].reshape(tm_count, 3, steps_dev).transpose(1, 0, 2).reshape(3, length)
    flat = flat.astype(jnp.float32)
    padded = jnp.concatenate([jnp.zeros((3, halo), jnp.float32), flat], 1)
    streams = bias[:, None] + taps[0][:, None] * padded[:, halo:]
    for offset in range(1, taps_count):
        streams = streams + taps[offset][:, None] * padded[:, halo - offset: halo - offset + length]
    streams = lax.reduce_precision(streams, 8, 7)
    gate_own = streams[0].reshape(tm_count, steps_dev)
    signal = lax.reduce_precision(streams[1] * streams[2], 8, 7).reshape(tm_count, steps_dev)
    convolved = long_conv(signal, h, tab)
    skip = lax.dynamic_index_in_dim(skip_gain, lax.axis_index("tm"), 0, keepdims=False)
    gated = ((convolved + skip * signal) * gate_own).astype(jnp.bfloat16)

    gated = lax.all_to_all(gated.reshape(tm_count, 2, -1), "tm", 0, 0, tiled=True)
    gated = gated.reshape(tm_count, steps_dev).T
    gated = gather_chan(gated)
    column_start = lax.axis_index("chan") * channels
    weight_cols = lax.dynamic_slice_in_dim(out_weight, column_start, channels, 1)
    mixed_out = jnp.dot(gated, weight_cols, preferred_element_type=jnp.float32) + out_bias
    return mixed_out.astype(jnp.bfloat16)


def solution(mesh):
    return jax.shard_map(
        shards,
        mesh=mesh,
        in_specs=(
            P("tm", "chan"),
            P(None, None, "chan"),
            P(None, "chan"),
            P(None, None, "chan"),
            P(None, "chan"),
            P(None, "tm", None, None, "chan"),
            P("chan"),
            P(),
            P("chan"),
        ),
        out_specs=P("tm", "chan"),
        check_vma=False,
    )
```

```python
import math

import jax
import jax.numpy as jnp
import numpy as np
from jax import lax
from jax.sharding import PartitionSpec as P

HI = lax.Precision.HIGH


def from_behind(array, axis, by):
    length = lax.axis_size(axis)
    pairs = [(i, i + by) for i in range(length) if 0 <= i + by < length]
    return lax.ppermute(array, axis, pairs)


def reverse_bits(values, digits):
    result = jnp.zeros_like(values)
    for bit_level in range(digits):
        result = result | (values >> bit_level & 1) << digits - 1 - bit_level
    return result


def dft_tables(tm_count, steps_dev):
    rows = 2 * tm_count
    digits = tm_count.bit_length() - 1
    r = lax.iota(jnp.int32, rows)
    k1 = 2 * reverse_bits(r // 2, digits) + r % 2
    m = lax.iota(jnp.int32, tm_count)
    t = lax.iota(jnp.int32, steps_dev)
    period = rows * steps_dev

    def turn(index, count):
        angle = (index % count).astype(jnp.float32) * (2 * math.pi / count)
        return jnp.cos(angle), jnp.sin(angle)

    c1, s1 = turn(k1[:, None] * m[None, :], rows)
    c2, s2 = turn(t[:, None] * t[None, :], steps_dev)
    ct, st = turn(k1[:, None] * t[None, :], period)
    c1, s1, c2, s2, ct, st = lax.optimization_barrier((c1, s1, c2, s2, ct, st))
    return dict(c1=c1, s1=s1, c2=c2, s2=s2, ct=ct, st=st, period=period)


def gather_chan(x):
    count = lax.axis_size("chan")
    wide = jnp.broadcast_to(x[:, None, :], (x.shape[0], count, x.shape[1]))
    return lax.all_to_all(wide, "chan", 1, 1, tiled=True).reshape(x.shape[0], count * x.shape[1])


def mm(a, b):
    return jnp.dot(a, b, precision=HI, preferred_element_type=jnp.float32)


def long_conv(x, h, tab):
    c1, s1, c2, s2, ct, st = (tab[k] for k in ("c1", "s1", "c2", "s2", "ct", "st"))
    ar = mm(c1, x)
    ai = -mm(s1, x)
    tr = ar * ct + ai * st
    ti = ai * ct - ar * st
    zr = mm(tr, c2) + mm(ti, s2)
    zi = mm(ti, c2) - mm(tr, s2)
    yr = h[0] * zr - h[1] * zi
    yi = h[0] * zi + h[1] * zr
    br = mm(yr, c2) - mm(yi, s2)
    bi = mm(yi, c2) + mm(yr, s2)
    ur = br * ct - bi * st
    ui = bi * ct + br * st
    y = lax.dot_general(c1, ur, (((0,), (0,)), ((), ())), precision=HI,
                        preferred_element_type=jnp.float32)
    y = y - lax.dot_general(s1, ui, (((0,), (0,)), ((), ())), precision=HI,
                            preferred_element_type=jnp.float32)
    return y * (1.0 / tab["period"])


def shards(series, proj_weight, proj_bias, short_taps, short_bias, spectrum,
           skip_gain, out_weight, out_bias):
    steps_dev = series.shape[0]
    model_width = proj_weight.shape[0]
    channels = proj_weight.shape[2]
    tm_count = lax.axis_size("tm")
    tab = dft_tables(tm_count, steps_dev)

    flat_weight = proj_weight.reshape(model_width, 3 * channels)
    taps_count = short_taps.shape[0]
    halo = taps_count - 1
    rows = gather_chan(series)
    projected = jnp.dot(rows, flat_weight, preferred_element_type=jnp.float32)
    projected = (projected.reshape(steps_dev, 3, channels) + proj_bias).astype(jnp.bfloat16)

    send = jnp.concatenate(
        [spectrum.reshape(-1, channels).astype(jnp.bfloat16),
         projected.transpose(1, 0, 2).reshape(3 * steps_dev, channels)], 0)
    send = send.T.reshape(channels, 2, -1)
    recv = lax.all_to_all(send, "tm", 0, 0, tiled=True).reshape(tm_count, -1)
    spec_len = spectrum.size // channels
    h = recv[:, :spec_len].astype(jnp.float32).reshape(tm_count, 2, spec_len // 2)
    h = jnp.stack([h[:, 0].reshape(2 * tm_count, steps_dev), h[:, 1].reshape(2 * tm_count, steps_dev)])
    own = lax.axis_index("tm")
    taps = lax.dynamic_index_in_dim(short_taps, own, 2, keepdims=False)
    bias = lax.dynamic_index_in_dim(short_bias, own, 1, keepdims=False)
    held = recv[:, spec_len:].astype(jnp.float32).reshape(tm_count, 3, steps_dev)

    def earlier(x, offset):
        carried = jnp.concatenate([jnp.zeros((1, offset), x.dtype), x[:-1, steps_dev - offset:]], 0)
        return jnp.concatenate([carried, x[:, :steps_dev - offset]], 1)

    streams = []
    for j in range(3):
        x = held[:, j]
        value = bias[j] + taps[0, j] * x
        for offset in range(1, taps_count):
            value = value + taps[offset, j] * earlier(x, offset)
        streams.append(lax.reduce_precision(value, 8, 7))
    gate_own = streams[0]
    signal = lax.reduce_precision(streams[1] * streams[2], 8, 7)
    convolved = long_conv(signal, h, tab)
    skip = lax.dynamic_index_in_dim(skip_gain, lax.axis_index("tm"), 0, keepdims=False)
    gated = ((convolved + skip * signal) * gate_own).astype(jnp.bfloat16)

    gated = lax.all_to_all(gated.reshape(tm_count, 2, -1), "tm", 0, 0, tiled=True)
    gated = gated.reshape(tm_count, steps_dev).T
    gated = gather_chan(gated)
    column_start = lax.axis_index("chan") * channels
    weight_cols = lax.dynamic_slice_in_dim(out_weight, column_start, channels, 1)
    mixed_out = jnp.dot(gated, weight_cols, preferred_element_type=jnp.float32) + out_bias
    return mixed_out.astype(jnp.bfloat16)


def solution(mesh):
    return jax.shard_map(
        shards,
        mesh=mesh,
        in_specs=(
            P("tm", "chan"),
            P(None, None, "chan"),
            P(None, "chan"),
            P(None, None, "chan"),
            P(None, "chan"),
            P(None, "tm", None, None, "chan"),
            P("chan"),
            P(),
            P("chan"),
        ),
        out_specs=P("tm", "chan"),
        check_vma=False,
    )
```

```python
import math

import jax
import jax.numpy as jnp
import numpy as np
from jax import lax
from jax.sharding import PartitionSpec as P

HI = lax.Precision.HIGH


def from_behind(array, axis, by):
    length = lax.axis_size(axis)
    pairs = [(i, i + by) for i in range(length) if 0 <= i + by < length]
    return lax.ppermute(array, axis, pairs)


def reverse_bits(values, digits):
    result = jnp.zeros_like(values)
    for bit_level in range(digits):
        result = result | (values >> bit_level & 1) << digits - 1 - bit_level
    return result


def dft_tables(tm_count, steps_dev):
    rows = 2 * tm_count
    digits = tm_count.bit_length() - 1
    r = lax.iota(jnp.int32, rows)
    k1 = 2 * reverse_bits(r // 2, digits) + r % 2
    m = lax.iota(jnp.int32, tm_count)
    t = lax.iota(jnp.int32, steps_dev)
    period = rows * steps_dev

    def turn(index, count):
        angle = (index % count).astype(jnp.float32) * (2 * math.pi / count)
        return jnp.cos(angle), jnp.sin(angle)

    c1, s1 = turn(k1[:, None] * m[None, :], rows)
    c2, s2 = turn(t[:, None] * t[None, :], steps_dev)
    ct, st = turn(k1[:, None] * t[None, :], period)
    c1, s1, c2, s2, ct, st = lax.optimization_barrier((c1, s1, c2, s2, ct, st))
    return dict(c1=c1, s1=s1, c2=c2, s2=s2, ct=ct, st=st, period=period)


def gather_chan(x):
    count = lax.axis_size("chan")
    wide = jnp.broadcast_to(x[:, None, :], (x.shape[0], count, x.shape[1]))
    return lax.all_to_all(wide, "chan", 1, 1, tiled=True).reshape(x.shape[0], count * x.shape[1])


def mm(a, b):
    return jnp.dot(a, b, precision=HI, preferred_element_type=jnp.float32)


def long_conv(x, h, tab):
    c1, s1, c2, s2, ct, st = (tab[k] for k in ("c1", "s1", "c2", "s2", "ct", "st"))
    ar = mm(c1, x)
    ai = -mm(s1, x)
    tr = ar * ct + ai * st
    ti = ai * ct - ar * st
    zr = mm(tr, c2) + mm(ti, s2)
    zi = mm(ti, c2) - mm(tr, s2)
    yr = h[0] * zr - h[1] * zi
    yi = h[0] * zi + h[1] * zr
    br = mm(yr, c2) - mm(yi, s2)
    bi = mm(yi, c2) + mm(yr, s2)
    ur = br * ct - bi * st
    ui = bi * ct + br * st
    y = lax.dot_general(c1, ur, (((0,), (0,)), ((), ())), precision=HI,
                        preferred_element_type=jnp.float32)
    y = y - lax.dot_general(s1, ui, (((0,), (0,)), ((), ())), precision=HI,
                            preferred_element_type=jnp.float32)
    return y * (1.0 / tab["period"])


def shards(series, proj_weight, proj_bias, short_taps, short_bias, spectrum,
           skip_gain, out_weight, out_bias):
    steps_dev = series.shape[0]
    model_width = proj_weight.shape[0]
    channels = proj_weight.shape[2]
    tm_count = lax.axis_size("tm")
    tab = dft_tables(tm_count, steps_dev)

    flat_weight = proj_weight.reshape(model_width, 3 * channels)
    taps_count = short_taps.shape[0]
    halo = taps_count - 1
    rows = gather_chan(series)
    projected = jnp.dot(rows, flat_weight, preferred_element_type=jnp.float32)
    projected = (projected.reshape(steps_dev, 3, channels) + proj_bias).astype(jnp.bfloat16)

    send = jnp.concatenate(
        [spectrum.reshape(-1, channels).astype(jnp.bfloat16),
         projected.transpose(1, 0, 2).reshape(3 * steps_dev, channels)], 0)
    send = send.T.reshape(channels, -1, 128)
    recv = lax.all_to_all(send, "tm", 0, 0, tiled=True).reshape(tm_count, -1)
    spec_len = spectrum.size // channels
    h = recv[:, :spec_len].astype(jnp.float32).reshape(tm_count, 2, spec_len // 2)
    h = jnp.stack([h[:, 0].reshape(2 * tm_count, steps_dev), h[:, 1].reshape(2 * tm_count, steps_dev)])
    own = lax.axis_index("tm")
    taps = lax.dynamic_index_in_dim(short_taps, own, 2, keepdims=False)
    bias = lax.dynamic_index_in_dim(short_bias, own, 1, keepdims=False)
    length = tm_count * steps_dev
    flat = recv[:, spec_len:].reshape(tm_count, 3, steps_dev).transpose(1, 0, 2).reshape(3, length)
    flat = flat.astype(jnp.float32)
    padded = jnp.concatenate([jnp.zeros((3, halo), jnp.float32), flat], 1)
    streams = bias[:, None] + taps[0][:, None] * padded[:, halo:]
    for offset in range(1, taps_count):
        streams = streams + taps[offset][:, None] * padded[:, halo - offset: halo - offset + length]
    streams = lax.reduce_precision(streams, 8, 7)
    gate_own = streams[0].reshape(tm_count, steps_dev)
    signal = lax.reduce_precision(streams[1] * streams[2], 8, 7).reshape(tm_count, steps_dev)
    convolved = long_conv(signal, h, tab)
    skip = lax.dynamic_index_in_dim(skip_gain, lax.axis_index("tm"), 0, keepdims=False)
    gated = ((convolved + skip * signal) * gate_own).astype(jnp.bfloat16)

    gated = lax.all_to_all(gated.reshape(tm_count, 2, -1), "tm", 0, 0, tiled=True)
    gated = gated.reshape(tm_count, steps_dev).T
    gated = gather_chan(gated)
    column_start = lax.axis_index("chan") * channels
    weight_cols = lax.dynamic_slice_in_dim(out_weight, column_start, channels, 1)
    mixed_out = jnp.dot(gated, weight_cols, preferred_element_type=jnp.float32) + out_bias
    return mixed_out.astype(jnp.bfloat16)


def solution(mesh):
    return jax.shard_map(
        shards,
        mesh=mesh,
        in_specs=(
            P("tm", "chan"),
            P(None, None, "chan"),
            P(None, "chan"),
            P(None, None, "chan"),
            P(None, "chan"),
            P(None, "tm", None, None, "chan"),
            P("chan"),
            P(),
            P("chan"),
        ),
        out_specs=P("tm", "chan"),
        check_vma=False,
    )
```

```python
import math

import jax
import jax.numpy as jnp
import numpy as np
from jax import lax
from jax.sharding import PartitionSpec as P

HI = lax.Precision.HIGH


def from_behind(array, axis, by):
    length = lax.axis_size(axis)
    pairs = [(i, i + by) for i in range(length) if 0 <= i + by < length]
    return lax.ppermute(array, axis, pairs)


def reverse_bits(values, digits):
    result = jnp.zeros_like(values)
    for bit_level in range(digits):
        result = result | (values >> bit_level & 1) << digits - 1 - bit_level
    return result


def dft_tables(tm_count, steps_dev):
    rows = 2 * tm_count
    digits = tm_count.bit_length() - 1
    r = lax.iota(jnp.int32, rows)
    k1 = 2 * reverse_bits(r // 2, digits) + r % 2
    m = lax.iota(jnp.int32, tm_count)
    t = lax.iota(jnp.int32, steps_dev)
    period = rows * steps_dev

    def turn(index, count):
        angle = (index % count).astype(jnp.float32) * (2 * math.pi / count)
        return jnp.cos(angle), jnp.sin(angle)

    c1, s1 = turn(k1[:, None] * m[None, :], rows)
    c2, s2 = turn(t[:, None] * t[None, :], steps_dev)
    ct, st = turn(k1[:, None] * t[None, :], period)
    c1, s1, c2, s2, ct, st = lax.optimization_barrier((c1, s1, c2, s2, ct, st))
    return dict(c1=c1, s1=s1, c2=c2, s2=s2, ct=ct, st=st, period=period)


def gather_chan(x):
    count = lax.axis_size("chan")
    wide = jnp.broadcast_to(x[:, None, :], (x.shape[0], count, x.shape[1]))
    return lax.all_to_all(wide, "chan", 1, 1, tiled=True).reshape(x.shape[0], count * x.shape[1])


def mm(a, b):
    return jnp.dot(a, b, precision=HI, preferred_element_type=jnp.float32)


def long_conv(x, h, tab):
    c1, s1, c2, s2, ct, st = (tab[k] for k in ("c1", "s1", "c2", "s2", "ct", "st"))
    ar = mm(c1, x)
    ai = -mm(s1, x)
    tr = ar * ct + ai * st
    ti = ai * ct - ar * st
    zr = mm(tr, c2) + mm(ti, s2)
    zi = mm(ti, c2) - mm(tr, s2)
    yr = h[0] * zr - h[1] * zi
    yi = h[0] * zi + h[1] * zr
    br = mm(yr, c2) - mm(yi, s2)
    bi = mm(yi, c2) + mm(yr, s2)
    ur = br * ct - bi * st
    ui = bi * ct + br * st
    y = lax.dot_general(c1, ur, (((0,), (0,)), ((), ())), precision=HI,
                        preferred_element_type=jnp.float32)
    y = y - lax.dot_general(s1, ui, (((0,), (0,)), ((), ())), precision=HI,
                            preferred_element_type=jnp.float32)
    return y * (1.0 / tab["period"])


def shards(series, proj_weight, proj_bias, short_taps, short_bias, spectrum,
           skip_gain, out_weight, out_bias):
    steps_dev = series.shape[0]
    model_width = proj_weight.shape[0]
    channels = proj_weight.shape[2]
    tm_count = lax.axis_size("tm")
    tab = dft_tables(tm_count, steps_dev)

    flat_weight = proj_weight.reshape(model_width, 3 * channels)
    taps_count = short_taps.shape[0]
    halo = taps_count - 1
    rows = gather_chan(series)
    projected = jnp.dot(rows, flat_weight, preferred_element_type=jnp.float32)
    projected = (projected.reshape(steps_dev, 3, channels) + proj_bias).astype(jnp.bfloat16)

    send = jnp.concatenate(
        [spectrum.reshape(-1, channels).astype(jnp.bfloat16),
         projected.transpose(1, 0, 2).reshape(3 * steps_dev, channels)], 0)
    send = send.T.reshape(channels, 2, -1)
    recv = lax.all_to_all(send, "tm", 0, 0, tiled=True).reshape(tm_count, -1)
    spec_len = spectrum.size // channels
    half = spec_len // 2
    h = [recv[:, part * half:(part + 1) * half].astype(jnp.float32).reshape(2 * tm_count, steps_dev)
         for part in range(2)]
    own = lax.axis_index("tm")
    taps = lax.dynamic_index_in_dim(short_taps, own, 2, keepdims=False)
    bias = lax.dynamic_index_in_dim(short_bias, own, 1, keepdims=False)
    length = tm_count * steps_dev
    flat = recv[:, spec_len:].reshape(tm_count, 3, steps_dev).transpose(1, 0, 2).reshape(3, length)
    flat = flat.astype(jnp.float32)
    padded = jnp.concatenate([jnp.zeros((3, halo), jnp.float32), flat], 1)
    streams = bias[:, None] + taps[0][:, None] * padded[:, halo:]
    for offset in range(1, taps_count):
        streams = streams + taps[offset][:, None] * padded[:, halo - offset: halo - offset + length]
    streams = lax.reduce_precision(streams, 8, 7)
    gate_own = streams[0].reshape(tm_count, steps_dev)
    signal = lax.reduce_precision(streams[1] * streams[2], 8, 7).reshape(tm_count, steps_dev)
    convolved = long_conv(signal, h, tab)
    skip = lax.dynamic_index_in_dim(skip_gain, lax.axis_index("tm"), 0, keepdims=False)
    gated = ((convolved + skip * signal) * gate_own).astype(jnp.bfloat16)

    gated = lax.all_to_all(gated.reshape(tm_count, 2, -1), "tm", 0, 0, tiled=True)
    gated = gated.reshape(tm_count, steps_dev).T
    gated = gather_chan(gated)
    column_start = lax.axis_index("chan") * channels
    weight_cols = lax.dynamic_slice_in_dim(out_weight, column_start, channels, 1)
    mixed_out = jnp.dot(gated, weight_cols, preferred_element_type=jnp.float32) + out_bias
    return mixed_out.astype(jnp.bfloat16)


def solution(mesh):
    return jax.shard_map(
        shards,
        mesh=mesh,
        in_specs=(
            P("tm", "chan"),
            P(None, None, "chan"),
            P(None, "chan"),
            P(None, None, "chan"),
            P(None, "chan"),
            P(None, "tm", None, None, "chan"),
            P("chan"),
            P(),
            P("chan"),
        ),
        out_specs=P("tm", "chan"),
        check_vma=False,
    )
```

```python
import math

import jax
import jax.numpy as jnp
import numpy as np
from jax import lax
from jax.sharding import PartitionSpec as P

HI = lax.Precision.HIGH


def from_behind(array, axis, by):
    length = lax.axis_size(axis)
    pairs = [(i, i + by) for i in range(length) if 0 <= i + by < length]
    return lax.ppermute(array, axis, pairs)


def reverse_bits(values, digits):
    result = jnp.zeros_like(values)
    for bit_level in range(digits):
        result = result | (values >> bit_level & 1) << digits - 1 - bit_level
    return result


def dft_tables(tm_count, steps_dev):
    rows = 2 * tm_count
    digits = tm_count.bit_length() - 1
    r = lax.iota(jnp.int32, rows)
    k1 = 2 * reverse_bits(r // 2, digits) + r % 2
    m = lax.iota(jnp.int32, tm_count)
    t = lax.iota(jnp.int32, steps_dev)
    period = rows * steps_dev

    def turn(index, count):
        angle = (index % count).astype(jnp.float32) * (2 * math.pi / count)
        return jnp.cos(angle), jnp.sin(angle)

    c1, s1 = turn(k1[:, None] * m[None, :], rows)
    c2, s2 = turn(t[:, None] * t[None, :], steps_dev)
    ct, st = turn(k1[:, None] * t[None, :], period)
    c1, s1, c2, s2, ct, st = lax.optimization_barrier((c1, s1, c2, s2, ct, st))
    return dict(c1=c1, s1=s1, c2=c2, s2=s2, ct=ct, st=st, period=period)


def gather_chan(x):
    count = lax.axis_size("chan")
    wide = jnp.broadcast_to(x[:, None, :], (x.shape[0], count, x.shape[1]))
    return lax.all_to_all(wide, "chan", 1, 1, tiled=True).reshape(x.shape[0], count * x.shape[1])


def mm(a, b):
    return jnp.dot(a, b, precision=HI, preferred_element_type=jnp.float32)


def long_conv(x, h, tab):
    c1, s1, c2, s2, ct, st = (tab[k] for k in ("c1", "s1", "c2", "s2", "ct", "st"))
    xb = x.astype(jnp.bfloat16)

    def mm_exact_rhs(a):
        high = a.astype(jnp.bfloat16)
        low = (a - high.astype(jnp.float32)).astype(jnp.bfloat16)
        return (jnp.dot(high, xb, preferred_element_type=jnp.float32)
                + jnp.dot(low, xb, preferred_element_type=jnp.float32))

    ar = mm_exact_rhs(c1)
    ai = -mm_exact_rhs(s1)
    tr = ar * ct + ai * st
    ti = ai * ct - ar * st
    zr = mm(tr, c2) + mm(ti, s2)
    zi = mm(ti, c2) - mm(tr, s2)
    yr = h[0] * zr - h[1] * zi
    yi = h[0] * zi + h[1] * zr
    br = mm(yr, c2) - mm(yi, s2)
    bi = mm(yi, c2) + mm(yr, s2)
    ur = br * ct - bi * st
    ui = bi * ct + br * st
    y = lax.dot_general(c1, ur, (((0,), (0,)), ((), ())), precision=HI,
                        preferred_element_type=jnp.float32)
    y = y - lax.dot_general(s1, ui, (((0,), (0,)), ((), ())), precision=HI,
                            preferred_element_type=jnp.float32)
    return y * (1.0 / tab["period"])


def shards(series, proj_weight, proj_bias, short_taps, short_bias, spectrum,
           skip_gain, out_weight, out_bias):
    steps_dev = series.shape[0]
    model_width = proj_weight.shape[0]
    channels = proj_weight.shape[2]
    tm_count = lax.axis_size("tm")
    tab = dft_tables(tm_count, steps_dev)

    flat_weight = proj_weight.reshape(model_width, 3 * channels)
    taps_count = short_taps.shape[0]
    halo = taps_count - 1
    rows = gather_chan(series)
    projected = jnp.dot(rows, flat_weight, preferred_element_type=jnp.float32)
    projected = (projected.reshape(steps_dev, 3, channels) + proj_bias).astype(jnp.bfloat16)

    send = jnp.concatenate(
        [spectrum.reshape(-1, channels).astype(jnp.bfloat16),
         projected.transpose(1, 0, 2).reshape(3 * steps_dev, channels)], 0)
    send = send.T.reshape(channels, 2, -1)
    recv = lax.all_to_all(send, "tm", 0, 0, tiled=True).reshape(tm_count, -1)
    spec_len = spectrum.size // channels
    half = spec_len // 2
    h = [recv[:, part * half:(part + 1) * half].astype(jnp.float32).reshape(2 * tm_count, steps_dev)
         for part in range(2)]
    own = lax.axis_index("tm")
    taps = lax.dynamic_index_in_dim(short_taps, own, 2, keepdims=False)
    bias = lax.dynamic_index_in_dim(short_bias, own, 1, keepdims=False)
    length = tm_count * steps_dev
    flat = recv[:, spec_len:].reshape(tm_count, 3, steps_dev).transpose(1, 0, 2).reshape(3, length)
    flat = flat.astype(jnp.float32)
    padded = jnp.concatenate([jnp.zeros((3, halo), jnp.float32), flat], 1)
    streams = bias[:, None] + taps[0][:, None] * padded[:, halo:]
    for offset in range(1, taps_count):
        streams = streams + taps[offset][:, None] * padded[:, halo - offset: halo - offset + length]
    streams = lax.reduce_precision(streams, 8, 7)
    gate_own = streams[0].reshape(tm_count, steps_dev)
    signal = lax.reduce_precision(streams[1] * streams[2], 8, 7).reshape(tm_count, steps_dev)
    convolved = long_conv(signal, h, tab)
    skip = lax.dynamic_index_in_dim(skip_gain, lax.axis_index("tm"), 0, keepdims=False)
    gated = ((convolved + skip * signal) * gate_own).astype(jnp.bfloat16)

    gated = lax.all_to_all(gated.reshape(tm_count, 2, -1), "tm", 0, 0, tiled=True)
    gated = gated.reshape(tm_count, steps_dev).T
    gated = gather_chan(gated)
    column_start = lax.axis_index("chan") * channels
    weight_cols = lax.dynamic_slice_in_dim(out_weight, column_start, channels, 1)
    mixed_out = jnp.dot(gated, weight_cols, preferred_element_type=jnp.float32) + out_bias
    return mixed_out.astype(jnp.bfloat16)


def solution(mesh):
    return jax.shard_map(
        shards,
        mesh=mesh,
        in_specs=(
            P("tm", "chan"),
            P(None, None, "chan"),
            P(None, "chan"),
            P(None, None, "chan"),
            P(None, "chan"),
            P(None, "tm", None, None, "chan"),
            P("chan"),
            P(),
            P("chan"),
        ),
        out_specs=P("tm", "chan"),
        check_vma=False,
    )
```
